1024 devices in a mesh: section: 64 (over x_hi, z, core), tp: 8 (over y), mirror: 2 (over x_lo).
Axes of the slice: x: 8 (x_hi: 4, x_lo: 2; x = x_hi * 2 + x_lo), y: 8, z: 8, core: 2. Of those that a mesh axis runs over, the one named last changes fastest.
Arguments:
- hidden: bfloat16 [2, 64, 2, 128, 14336], P(None, 'section', 'mirror', None, 'tp'), may hold values from -6 to 6
- incoming: bfloat16 [2, 64, 2, 128, 4096], P(None, 'section', 'mirror', None, 'tp'), may hold values from -0.3984375 to 0.3984375
- block_mask: int32 [32, 112, 32], P(None, 'tp'), may hold values from 0 to 1, as said below
Outputs:
- block_grads: bfloat16 [64, 8, 126, 128, 128], P('section', 'tp', 'mirror')
The draws below stay inside these ranges and needn't reach their ends.
Inputs may be any that keep to these rules, and one draw needn't show every extreme that they name: `block_mask`: for every section and every index of tp, its 14 block rows keep between 7/16 and 9/16 of their blocks, at most 252; in every section exactly 252 on some index of tp.
All inputs are finite; a program needn't handle non-finite values.
Results may differ from the reference program's by a relative error of at most 0.006.
Values may be sent and summed in bfloat16 or wider, within the bound.
No kernel may reach another device: no remote copies, remote signals or barrier semaphores. Data moves between devices by JAX's collectives and lax.ppermute only.
A program may use at most 64 MiB of HBM per device.

```python
import jax
import jax.numpy as jnp
from jax import lax

D = 4096
FF = 14336
BLK = 128
ROWS = 128
NSTG = 32
FFB = 14
DB = 32
KCAP = 252
N_SECTION = 64
N_TP = 8
N_MIRROR = 2


def draw_block_mask(key, part):
    blocks = FFB * DB
    key_counts = jax.random.fold_in(key, 11)
    key_busiest = jax.random.fold_in(key, 12)
    key_scores = jax.random.fold_in(key, 13)
    counts_base = jax.random.randint(key_counts, (NSTG, N_TP), blocks * 7 // 16, KCAP + 1)
    busiest = jax.random.randint(key_busiest, (NSTG,), 0, N_TP)
    counts = jnp.where(jnp.arange(N_TP)[None, :] == busiest[:, None], KCAP, counts_base)
    scores = jax.random.randint(key_scores, (NSTG, N_TP, blocks), 0, 1 << 20) * blocks + jnp.arange(blocks)[None, None, :]
    ordering = jnp.argsort(scores, axis=-1, stable=True)
    rank_table = jnp.argsort(ordering, axis=-1, stable=True)
    kept_flags = (rank_table < counts[:, :, None]).astype(jnp.int32)
    return kept_flags.reshape(NSTG, N_TP * FFB, DB)


def level_of(key, extent, cuts, low, top_value):
    factor_of = 1.0
    for dim, parts in cuts:
        draws = jax.random.uniform(jax.random.fold_in(jax.random.fold_in(key, 6), dim), (parts,), jnp.float32, low / len(cuts), top_value / len(cuts))
        factor_of = factor_of * jnp.repeat(jnp.exp(draws), extent[dim] // parts).reshape((-1,) + (1,) * (len(extent) - 1 - dim))
    return factor_of


def gaussian(rng, shape, width, limit, shards=(), kind=jnp.bfloat16):
    loudness = level_of(rng, shape, shards, -0.22, 0.18) if shards else 1.0
    array = jax.random.normal(rng, shape, jnp.float32) * width * loudness
    return jnp.minimum(jnp.maximum(array, -limit), limit).astype(kind)


def setup_inputs(seed: int = 0) -> dict:
    seeds = jax.random.split(jax.random.key(seed), 4)
    hidden = gaussian(seeds[0], (2, N_SECTION, N_MIRROR, ROWS, FF), 1.0, 6.0, ((1, 64), (2, 2), (4, 8)))
    incoming = gaussian(seeds[1], (2, N_SECTION, N_MIRROR, ROWS, D), 0.05, 0.3984375, ((1, 64), (2, 2), (4, 8)))
    block_mask = draw_block_mask(jax.random.fold_in(seeds[3], 71), 0)
    return dict(hidden=hidden, incoming=incoming, block_mask=block_mask)


def slot_table(mask_local, slot_total):
    flat = mask_local.reshape(-1).astype(jnp.int32)
    running = jnp.cumsum(flat).astype(jnp.int32)
    positions = jnp.arange(slot_total, dtype=jnp.int32)
    targets = jnp.sum((running[None, :] <= positions[:, None]).astype(jnp.int32), axis=1).astype(jnp.int32)
    usable = positions < running[-1]
    targets = jnp.minimum(targets, flat.shape[0] - 1).astype(jnp.int32)
    columns_count = mask_local.shape[1]
    return (targets // columns_count).astype(jnp.int32), (targets % columns_count).astype(jnp.int32), usable


def block_partials(hidden_rows, cotangent, block_rows, block_cols, usable):
    row_total = hidden_rows.shape[0]
    hidden_blocks = hidden_rows.astype(jnp.float32).reshape(row_total, -1, BLK)
    cot_blocks = cotangent.astype(jnp.float32).reshape(row_total, -1, BLK)
    left = jnp.take(hidden_blocks, block_rows, axis=1)
    right = jnp.take(cot_blocks, block_cols, axis=1)
    product = jnp.einsum('nkc,nkd->kcd', left, right)
    product = jnp.where(usable[:, None, None], product, jnp.zeros_like(product))
    return product.astype(jnp.bfloat16)


def reference(hidden, incoming, block_mask):
    arrived_down = jnp.roll(incoming[0], -1, axis=0)
    arrived_up = jnp.roll(incoming[1], 1, axis=0)
    arrived = jnp.stack([arrived_down, arrived_up])
    ff_shard = FF // N_TP

    def section_shard(index):
        section_id = (index // N_TP).astype(jnp.int32)
        shard = (index % N_TP).astype(jnp.int32)
        mask_local = lax.dynamic_slice(block_mask, (section_id, shard * FFB, jnp.int32(0)), (1, FFB, DB))[0]
        block_rows, block_cols, usable = slot_table(mask_local, KCAP)
        replica_sums = []
        for mirror_id in range(N_MIRROR):
            replica_terms = []
            for half_index in range(2):
                position = section_id + half_index * NSTG
                hidden_rows = lax.dynamic_slice(hidden, (jnp.int32(0), position, jnp.int32(mirror_id), jnp.int32(0), shard * ff_shard), (2, 1, 1, ROWS, ff_shard)).reshape(2 * ROWS, ff_shard)
                cotangent = lax.dynamic_slice(arrived, (jnp.int32(0), position, jnp.int32(mirror_id), jnp.int32(0), jnp.int32(0)), (2, 1, 1, ROWS, D)).reshape(2 * ROWS, D)
                replica_terms.append(block_partials(hidden_rows, cotangent, block_rows, block_cols, usable))
            paired = (replica_terms[0].astype(jnp.float32) + replica_terms[1].astype(jnp.float32)).astype(jnp.bfloat16)
            replica_sums.append(paired)
        return (replica_sums[0].astype(jnp.float32) + replica_sums[1].astype(jnp.float32)).astype(jnp.bfloat16)

    grads = lax.map(section_shard, jnp.arange(NSTG * N_TP, dtype=jnp.int32))
    grads = grads.reshape(NSTG, N_TP, 2, KCAP // 2, BLK, BLK)
    grads = jnp.transpose(grads, (2, 0, 1, 3, 4, 5)).reshape(N_SECTION, N_TP, KCAP // 2, BLK, BLK)
    return grads
```

```python
import jax
import jax.numpy as jnp
from jax import lax
from jax.sharding import PartitionSpec as P

BLK = 128


def passed_along(block, axis, distance):
    devices = range(lax.axis_size(axis))
    route = [((i - distance) % len(devices), i) for i in devices]
    return lax.ppermute(block, axis, route)


def from_partner(value, axis, apart):
    mask = 2**apart
    pairs = [(source, source ^ mask) for source in range(lax.axis_size(axis))]
    return lax.ppermute(value, axis, pairs)


def slot_table(mask_local, slot_total):
    flat = mask_local.reshape(-1)
    running = jnp.cumsum(flat)
    positions = jnp.arange(slot_total, dtype=jnp.int32)
    targets = jnp.sum((running[None, :] <= positions[:, None]).astype(jnp.int32), axis=1)
    usable = positions < running[-1]
    targets = jnp.minimum(targets, flat.shape[0] - 1)
    columns_count = mask_local.shape[1]
    return (targets // columns_count, targets % columns_count, usable)


def body(hidden, incoming, block_mask):
    sections_total = lax.axis_size("section")
    half_count = sections_total // 2
    position = lax.axis_index("section")
    half_index = position // half_count
    section_index = position % half_count
    swap_bit = sections_total.bit_length() - 2
    block_side = BLK
    row_count = hidden.shape[3]
    ff_local = hidden.shape[4]

    own_hidden = hidden[:, 0, 0].reshape(2 * row_count, ff_local)
    partner_hidden = from_partner(own_hidden, "section", swap_bit)
    down_part = passed_along(incoming[0, 0, 0], "section", -1)
    up_part = passed_along(incoming[1, 0, 0], "section", 1)
    own_arrived = jnp.stack([down_part, up_part])
    partner_arrived = from_partner(own_arrived, "section", swap_bit)
    own_cot = lax.all_gather(own_arrived, "tp", axis=2, tiled=True)
    partner_cot = lax.all_gather(partner_arrived, "tp", axis=2, tiled=True)
    d_total = own_cot.shape[2]
    cot = jnp.concatenate(
        [own_cot.reshape(2 * row_count, d_total), partner_cot.reshape(2 * row_count, d_total)], axis=0
    )
    hidden_rows = jnp.concatenate([own_hidden, partner_hidden], axis=0)

    ffb = ff_local // block_side
    db = d_total // block_side
    dense = jnp.einsum(
        "nic,njd->ijcd",
        hidden_rows.reshape(-1, ffb, block_side),
        cot.reshape(-1, db, block_side),
        preferred_element_type=jnp.float32,
    ).astype(jnp.bfloat16)

    mask_local = lax.dynamic_index_in_dim(block_mask, section_index, 0, keepdims=False)
    slot_total = mask_local.shape[0] * mask_local.shape[1] * 9 // 16
    slots_half = slot_total // 2
    block_rows, block_cols, usable = slot_table(mask_local, slot_total)
    rows_h = lax.dynamic_slice_in_dim(block_rows, half_index * slots_half, slots_half, 0)
    cols_h = lax.dynamic_slice_in_dim(block_cols, half_index * slots_half, slots_half, 0)
    usable_h = lax.dynamic_slice_in_dim(usable, half_index * slots_half, slots_half, 0)
    flat_index = rows_h * db + cols_h
    picked = jnp.take(dense.reshape(ffb * db, block_side, block_side), flat_index, axis=0)
    paired = jnp.where(usable_h[:, None, None], picked, jnp.zeros_like(picked))
    summed = lax.psum_scatter(paired, "mirror", scatter_dimension=0, tiled=True)
    return summed.reshape(1, 1, -1, block_side, block_side)


def solution(mesh):
    placed = (
        P(None, "section", "mirror", None, "tp"),
        P(None, "section", "mirror", None, "tp"),
        P(None, "tp", None),
    )
    return jax.shard_map(
        body,
        mesh=mesh,
        in_specs=placed,
        out_specs=P("section", "tp", "mirror", None, None),
        check_vma=False,
    )
```

```python
import jax
import jax.numpy as jnp
from jax import lax
from jax.sharding import PartitionSpec as P

BLK = 128


def passed_along(block, axis, distance):
    devices = range(lax.axis_size(axis))
    route = [((i - distance) % len(devices), i) for i in devices]
    return lax.ppermute(block, axis, route)


def from_partner(value, axis, apart):
    mask = 2**apart
    pairs = [(source, source ^ mask) for source in range(lax.axis_size(axis))]
    return lax.ppermute(value, axis, pairs)


def slot_table(mask_local, slot_total):
    flat = mask_local.reshape(-1)
    running = jnp.cumsum(flat)
    positions = jnp.arange(slot_total, dtype=jnp.int32)
    targets = jnp.sum((running[None, :] <= positions[:, None]).astype(jnp.int32), axis=1)
    usable = positions < running[-1]
    targets = jnp.minimum(targets, flat.shape[0] - 1)
    columns_count = mask_local.shape[1]
    return (targets // columns_count, targets % columns_count, usable)


def body(hidden, incoming, block_mask):
    sections_total = lax.axis_size("section")
    half_count = sections_total // 2
    position = lax.axis_index("section")
    half_index = position // half_count
    section_index = position % half_count
    swap_bit = sections_total.bit_length() - 2
    block_side = BLK
    row_count = hidden.shape[3]
    ff_local = hidden.shape[4]

    own_hidden = hidden[:, 0, 0].reshape(2 * row_count, ff_local)
    partner_hidden = from_partner(own_hidden, "section", swap_bit)
    down_part = passed_along(incoming[0, 0, 0], "section", -1)
    up_part = passed_along(incoming[1, 0, 0], "section", 1)
    own_arrived = jnp.stack([down_part, up_part])
    partner_arrived = from_partner(own_arrived, "section", swap_bit)
    own_cot = lax.all_gather(own_arrived, "tp", axis=2, tiled=True)
    partner_cot = lax.all_gather(partner_arrived, "tp", axis=2, tiled=True)
    d_total = own_cot.shape[2]
    ffb = ff_local // block_side
    db = d_total // block_side

    mask_local = lax.dynamic_index_in_dim(block_mask, section_index, 0, keepdims=False)
    slot_total = mask_local.shape[0] * mask_local.shape[1] * 9 // 16
    slots_half = slot_total // 2
    slots_quarter = slots_half // 2
    block_rows, block_cols, usable = slot_table(mask_local, slot_total)
    mirror_index = lax.axis_index("mirror")

    def quarter(which):
        start = half_index * slots_half + which * slots_quarter
        pick = lambda table: lax.dynamic_slice_in_dim(table, start, slots_quarter, 0)
        return pick(block_rows), pick(block_cols), pick(usable)

    sent_q = quarter(1 - mirror_index)
    kept_q = quarter(mirror_index)

    def partial_of(hidden_rows, cot_rows):
        return jnp.einsum(
            "njd,nic->jidc",
            cot_rows.reshape(-1, db, block_side),
            hidden_rows.reshape(-1, ffb, block_side),
            preferred_element_type=jnp.float32,
        ).astype(jnp.bfloat16)

    def blocks_of(dense, table):
        rows_q, cols_q, usable_q = table
        picked = jnp.swapaxes(dense[cols_q, rows_q], 1, 2).astype(jnp.float32)
        return jnp.where(usable_q[:, None, None], picked, 0.0)

    own_dense = partial_of(own_hidden, own_cot)
    partner_dense = partial_of(partner_hidden, partner_cot)

    def paired_of(table):
        total = blocks_of(own_dense, table) + blocks_of(partner_dense, table)
        return total.astype(jnp.bfloat16)

    outgoing = paired_of(sent_q)
    received = from_partner(outgoing, "mirror", 0)
    kept = paired_of(kept_q)
    summed = (kept.astype(jnp.float32) + received.astype(jnp.float32)).astype(jnp.bfloat16)
    return summed.reshape(1, 1, -1, block_side, block_side)


def solution(mesh):
    placed = (
        P(None, "section", "mirror", None, "tp"),
        P(None, "section", "mirror", None, "tp"),
        P(None, "tp", None),
    )
    return jax.shard_map(
        body,
        mesh=mesh,
        in_specs=placed,
        out_specs=P("section", "tp", "mirror", None, None),
        check_vma=False,
    )
```

```python
import jax
import jax.numpy as jnp
from jax import lax
from jax.sharding import PartitionSpec as P

BLK = 128


def passed_along(block, axis, distance):
    devices = range(lax.axis_size(axis))
    route = [((i - distance) % len(devices), i) for i in devices]
    return lax.ppermute(block, axis, route)


def from_partner(value, axis, apart):
    mask = 2**apart
    pairs = [(source, source ^ mask) for source in range(lax.axis_size(axis))]
    return lax.ppermute(value, axis, pairs)


def slot_table(mask_local, slot_total):
    flat = mask_local.reshape(-1)
    running = jnp.cumsum(flat)
    positions = jnp.arange(slot_total, dtype=jnp.int32)
    targets = jnp.sum((running[None, :] <= positions[:, None]).astype(jnp.int32), axis=1)
    usable = positions < running[-1]
    targets = jnp.minimum(targets, flat.shape[0] - 1)
    columns_count = mask_local.shape[1]
    return (targets // columns_count, targets % columns_count, usable)


def body(hidden, incoming, block_mask):
    sections_total = lax.axis_size("section")
    half_count = sections_total // 2
    position = lax.axis_index("section")
    half_index = position // half_count
    section_index = position % half_count
    swap_bit = sections_total.bit_length() - 2
    block_side = BLK
    row_count = hidden.shape[3]
    ff_local = hidden.shape[4]

    own_hidden = hidden[:, 0, 0].reshape(2 * row_count, ff_local)
    partner_hidden = from_partner(own_hidden, "section", swap_bit)
    down_part = passed_along(incoming[0, 0, 0], "section", -1)
    up_part = passed_along(incoming[1, 0, 0], "section", 1)
    own_arrived = jnp.stack([down_part, up_part])
    partner_arrived = from_partner(own_arrived, "section", swap_bit)
    own_incoming_all = lax.all_gather(incoming[:, 0, 0], "tp", axis=2, tiled=True)
    own_cot = jnp.stack(
        [
            passed_along(own_incoming_all[0], "section", -1),
            passed_along(own_incoming_all[1], "section", 1),
        ]
    )
    partner_cot = lax.all_gather(partner_arrived, "tp", axis=2, tiled=True)
    d_total = own_cot.shape[2]
    ffb = ff_local // block_side
    db = d_total // block_side

    mask_local = lax.dynamic_index_in_dim(block_mask, section_index, 0, keepdims=False)
    slot_total = mask_local.shape[0] * mask_local.shape[1] * 9 // 16
    slots_half = slot_total // 2
    slots_quarter = slots_half // 2
    block_rows, block_cols, usable = slot_table(mask_local, slot_total)
    mirror_index = lax.axis_index("mirror")

    def quarter(which):
        start = half_index * slots_half + which * slots_quarter
        pick = lambda table: lax.dynamic_slice_in_dim(table, start, slots_quarter, 0)
        return pick(block_rows), pick(block_cols), pick(usable)

    sent_q = quarter(1 - mirror_index)
    kept_q = quarter(mirror_index)

    def partial_of(hidden_rows, cot_rows):
        return jnp.einsum(
            "njd,nic->jidc",
            cot_rows.reshape(-1, db, block_side),
            hidden_rows.reshape(-1, ffb, block_side),
            preferred_element_type=jnp.float32,
        ).astype(jnp.bfloat16)

    def blocks_of(dense, table):
        rows_q, cols_q, usable_q = table
        picked = jnp.swapaxes(dense[cols_q, rows_q], 1, 2).astype(jnp.float32)
        return jnp.where(usable_q[:, None, None], picked, 0.0)

    own_dense = partial_of(own_hidden, own_cot)
    partner_dense = partial_of(partner_hidden, partner_cot)

    def paired_of(table):
        total = blocks_of(own_dense, table) + blocks_of(partner_dense, table)
        return total.astype(jnp.bfloat16)

    outgoing = paired_of(sent_q)
    received = from_partner(outgoing, "mirror", 0)
    kept = paired_of(kept_q)
    summed = (kept.astype(jnp.float32) + received.astype(jnp.float32)).astype(jnp.bfloat16)
    return summed.reshape(1, 1, -1, block_side, block_side)


def solution(mesh):
    placed = (
        P(None, "section", "mirror", None, "tp"),
        P(None, "section", "mirror", None, "tp"),
        P(None, "tp", None),
    )
    return jax.shard_map(
        body,
        mesh=mesh,
        in_specs=placed,
        out_specs=P("section", "tp", "mirror", None, None),
        check_vma=False,
    )
```

```python
import jax
import jax.numpy as jnp
from jax import lax
from jax.sharding import PartitionSpec as P

BLK = 128


def passed_along(block, axis, distance):
    devices = range(lax.axis_size(axis))
    route = [((i - distance) % len(devices), i) for i in devices]
    return lax.ppermute(block, axis, route)


def from_partner(value, axis, apart):
    mask = 2**apart
    pairs = [(source, source ^ mask) for source in range(lax.axis_size(axis))]
    return lax.ppermute(value, axis, pairs)


def slot_table(mask_local, slot_total):
    flat = mask_local.reshape(-1)
    running = jnp.cumsum(flat)
    positions = jnp.arange(slot_total, dtype=jnp.int32)
    targets = jnp.sum((running[None, :] <= positions[:, None]).astype(jnp.int32), axis=1)
    usable = positions < running[-1]
    targets = jnp.minimum(targets, flat.shape[0] - 1)
    columns_count = mask_local.shape[1]
    return (targets // columns_count, targets % columns_count, usable)


def body(hidden, incoming, block_mask):
    sections_total = lax.axis_size("section")
    half_count = sections_total // 2
    position = lax.axis_index("section")
    half_index = position // half_count
    section_index = position % half_count
    swap_bit = sections_total.bit_length() - 2
    block_side = BLK
    row_count = hidden.shape[3]
    ff_local = hidden.shape[4]

    own_hidden = hidden[:, 0, 0].reshape(2 * row_count, ff_local)
    partner_hidden = from_partner(own_hidden, "section", swap_bit)
    down_part = passed_along(incoming[0, 0, 0], "section", -1)
    up_part = passed_along(incoming[1, 0, 0], "section", 1)
    own_arrived = jnp.stack([down_part, up_part])
    partner_arrived = from_partner(own_arrived, "section", swap_bit)
    own_incoming_all = lax.all_gather(incoming[:, 0, 0], "tp", axis=2, tiled=True)
    own_cot = jnp.stack(
        [
            passed_along(own_incoming_all[0], "section", -1),
            passed_along(own_incoming_all[1], "section", 1),
        ]
    )
    partner_cot = lax.all_gather(partner_arrived, "tp", axis=2, tiled=True)
    d_total = own_cot.shape[2]
    ffb = ff_local // block_side
    db = d_total // block_side

    mask_local = lax.dynamic_index_in_dim(block_mask, section_index, 0, keepdims=False)
    slot_total = mask_local.shape[0] * mask_local.shape[1] * 9 // 16
    slots_half = slot_total // 2
    slots_quarter = slots_half // 2
    block_rows, block_cols, usable = slot_table(mask_local, slot_total)
    mirror_index = lax.axis_index("mirror")

    def quarter(which):
        start = half_index * slots_half + which * slots_quarter
        pick = lambda table: lax.dynamic_slice_in_dim(table, start, slots_quarter, 0)
        return pick(block_rows), pick(block_cols), pick(usable)

    sent_q = quarter(1 - mirror_index)
    kept_q = quarter(mirror_index)

    def partial_of(hidden_rows, cot_rows):
        return jnp.einsum(
            "njd,nic->jidc",
            cot_rows.reshape(-1, db, block_side),
            hidden_rows.reshape(-1, ffb, block_side),
            preferred_element_type=jnp.float32,
        ).astype(jnp.bfloat16)

    def blocks_of(dense, table):
        rows_q, cols_q, usable_q = table
        picked = jnp.swapaxes(dense[cols_q, rows_q], 1, 2)
        return jnp.where(usable_q[:, None, None], picked, jnp.zeros_like(picked))

    own_dense = partial_of(own_hidden, own_cot)
    own_sent = blocks_of(own_dense, sent_q)
    own_kept = blocks_of(own_dense, kept_q)
    own_sent, own_kept, partner_cot = lax.optimization_barrier((own_sent, own_kept, partner_cot))
    partner_dense = partial_of(partner_hidden, partner_cot)

    def paired_of(own_blocks, table):
        total = own_blocks.astype(jnp.float32) + blocks_of(partner_dense, table).astype(jnp.float32)
        return total.astype(jnp.bfloat16)

    outgoing = paired_of(own_sent, sent_q)
    received = from_partner(outgoing, "mirror", 0)
    kept = paired_of(own_kept, kept_q)
    summed = (kept.astype(jnp.float32) + received.astype(jnp.float32)).astype(jnp.bfloat16)
    return summed.reshape(1, 1, -1, block_side, block_side)


def solution(mesh):
    placed = (
        P(None, "section", "mirror", None, "tp"),
        P(None, "section", "mirror", None, "tp"),
        P(None, "tp", None),
    )
    return jax.shard_map(
        body,
        mesh=mesh,
        in_specs=placed,
        out_specs=P("section", "tp", "mirror", None, None),
        check_vma=False,
    )
```

```python
import jax
import jax.numpy as jnp
from jax import lax
from jax.sharding import PartitionSpec as P

BLK = 128


def passed_along(block, axis, distance):
    devices = range(lax.axis_size(axis))
    route = [((i - distance) % len(devices), i) for i in devices]
    return lax.ppermute(block, axis, route)


def from_partner(value, axis, apart):
    mask = 2**apart
    pairs = [(source, source ^ mask) for source in range(lax.axis_size(axis))]
    return lax.ppermute(value, axis, pairs)


def gathered_by_permutes(value, axis):
    count = lax.axis_size(axis)
    pieces = jnp.stack([value] + [passed_along(value, axis, shift) for shift in range(1, count)])
    order = (lax.axis_index(axis) - jnp.arange(count, dtype=jnp.int32)) % count
    placed = jnp.take(pieces, order, axis=0)
    placed = jnp.moveaxis(placed, 0, -2)
    return placed.reshape(placed.shape[:-2] + (count * value.shape[-1],))


def slot_table(mask_local, slot_total):
    flat = mask_local.reshape(-1)
    running = jnp.cumsum(flat)
    positions = jnp.arange(slot_total, dtype=jnp.int32)
    targets = jnp.sum((running[None, :] <= positions[:, None]).astype(jnp.int32), axis=1)
    usable = positions < running[-1]
    targets = jnp.minimum(targets, flat.shape[0] - 1)
    columns_count = mask_local.shape[1]
    return (targets // columns_count, targets % columns_count, usable)


def body(hidden, incoming, block_mask):
    sections_total = lax.axis_size("section")
    half_count = sections_total // 2
    position = lax.axis_index("section")
    half_index = position // half_count
    section_index = position % half_count
    swap_bit = sections_total.bit_length() - 2
    block_side = BLK
    row_count = hidden.shape[3]
    ff_local = hidden.shape[4]

    own_hidden = hidden[:, 0, 0].reshape(2 * row_count, ff_local)
    partner_hidden = from_partner(own_hidden, "section", swap_bit)
    down_part = passed_along(incoming[0, 0, 0], "section", -1)
    up_part = passed_along(incoming[1, 0, 0], "section", 1)
    own_arrived = jnp.stack([down_part, up_part])
    partner_arrived = from_partner(own_arrived, "section", swap_bit)
    own_cot = lax.all_gather(own_arrived, "tp", axis=2, tiled=True)
    partner_cot = gathered_by_permutes(partner_arrived, "tp")
    d_total = own_cot.shape[2]
    ffb = ff_local // block_side
    db = d_total // block_side

    mask_local = lax.dynamic_index_in_dim(block_mask, section_index, 0, keepdims=False)
    slot_total = mask_local.shape[0] * mask_local.shape[1] * 9 // 16
    slots_half = slot_total // 2
    slots_quarter = slots_half // 2
    block_rows, block_cols, usable = slot_table(mask_local, slot_total)
    mirror_index = lax.axis_index("mirror")

    def quarter(which):
        start = half_index * slots_half + which * slots_quarter
        pick = lambda table: lax.dynamic_slice_in_dim(table, start, slots_quarter, 0)
        return pick(block_rows), pick(block_cols), pick(usable)

    sent_q = quarter(1 - mirror_index)
    kept_q = quarter(mirror_index)

    def partial_of(hidden_rows, cot_rows):
        return jnp.einsum(
            "njd,nic->jidc",
            cot_rows.reshape(-1, db, block_side),
            hidden_rows.reshape(-1, ffb, block_side),
            preferred_element_type=jnp.float32,
        ).astype(jnp.bfloat16)

    def blocks_of(dense, table):
        rows_q, cols_q, usable_q = table
        picked = jnp.swapaxes(dense[cols_q, rows_q], 1, 2)
        return jnp.where(usable_q[:, None, None], picked, jnp.zeros_like(picked))

    own_dense = partial_of(own_hidden, own_cot)
    own_sent = blocks_of(own_dense, sent_q)
    own_kept = blocks_of(own_dense, kept_q)
    own_sent, own_kept, partner_cot = lax.optimization_barrier((own_sent, own_kept, partner_cot))
    partner_dense = partial_of(partner_hidden, partner_cot)

    def paired_of(own_blocks, table):
        total = own_blocks.astype(jnp.float32) + blocks_of(partner_dense, table).astype(jnp.float32)
        return total.astype(jnp.bfloat16)

    outgoing = paired_of(own_sent, sent_q)
    received = from_partner(outgoing, "mirror", 0)
    kept = paired_of(own_kept, kept_q)
    summed = (kept.astype(jnp.float32) + received.astype(jnp.float32)).astype(jnp.bfloat16)
    return summed.reshape(1, 1, -1, block_side, block_side)


def solution(mesh):
    placed = (
        P(None, "section", "mirror", None, "tp"),
        P(None, "section", "mirror", None, "tp"),
        P(None, "tp", None),
    )
    return jax.shard_map(
        body,
        mesh=mesh,
        in_specs=placed,
        out_specs=P("section", "tp", "mirror", None, None),
        check_vma=False,
    )
```

```python
import jax
import jax.numpy as jnp
from jax import lax
from jax.sharding import PartitionSpec as P

BLK = 128


def passed_along(block, axis, distance):
    devices = range(lax.axis_size(axis))
    route = [((i - distance) % len(devices), i) for i in devices]
    return lax.ppermute(block, axis, route)


def from_partner(value, axis, apart):
    mask = 2**apart
    pairs = [(source, source ^ mask) for source in range(lax.axis_size(axis))]
    return lax.ppermute(value, axis, pairs)


def slot_table(mask_local, slot_total):
    flat = mask_local.reshape(-1)
    running = jnp.cumsum(flat)
    positions = jnp.arange(slot_total, dtype=jnp.int32)
    targets = jnp.sum((running[None, :] <= positions[:, None]).astype(jnp.int32), axis=1)
    usable = positions < running[-1]
    targets = jnp.minimum(targets, flat.shape[0] - 1)
    columns_count = mask_local.shape[1]
    return (targets // columns_count, targets % columns_count, usable)


def body(hidden, incoming, block_mask):
    sections_total = lax.axis_size("section")
    half_count = sections_total // 2
    position = lax.axis_index("section")
    half_index = position // half_count
    section_index = position % half_count
    swap_bit = sections_total.bit_length() - 2
    block_side = BLK
    row_count = hidden.shape[3]
    ff_local = hidden.shape[4]

    own_hidden = hidden[:, 0, 0].reshape(2 * row_count, ff_local)
    partner_hidden = from_partner(own_hidden, "section", swap_bit)
    down_part = passed_along(incoming[0, 0, 0], "section", -1)
    up_part = passed_along(incoming[1, 0, 0], "section", 1)
    own_arrived = jnp.stack([down_part, up_part])
    partner_arrived = from_partner(own_arrived, "section", swap_bit)
    own_cot = lax.all_gather(own_arrived, "tp", axis=2, tiled=True)
    partner_down = lax.all_gather(partner_arrived[0], "tp", axis=1, tiled=True)
    partner_up = from_partner(own_cot[1], "section", swap_bit)
    partner_cot = jnp.stack([partner_down, partner_up])
    d_total = own_cot.shape[2]
    ffb = ff_local // block_side
    db = d_total // block_side

    mask_local = lax.dynamic_index_in_dim(block_mask, section_index, 0, keepdims=False)
    slot_total = mask_local.shape[0] * mask_local.shape[1] * 9 // 16
    slots_half = slot_total // 2
    slots_quarter = slots_half // 2
    block_rows, block_cols, usable = slot_table(mask_local, slot_total)
    mirror_index = lax.axis_index("mirror")

    def quarter(which):
        start = half_index * slots_half + which * slots_quarter
        pick = lambda table: lax.dynamic_slice_in_dim(table, start, slots_quarter, 0)
        return pick(block_rows), pick(block_cols), pick(usable)

    sent_q = quarter(1 - mirror_index)
    kept_q = quarter(mirror_index)

    def partial_of(hidden_rows, cot_rows):
        return jnp.einsum(
            "njd,nic->jidc",
            cot_rows.reshape(-1, db, block_side),
            hidden_rows.reshape(-1, ffb, block_side),
            preferred_element_type=jnp.float32,
        ).astype(jnp.bfloat16)

    def blocks_of(dense, table):
        rows_q, cols_q, usable_q = table
        picked = jnp.swapaxes(dense[cols_q, rows_q], 1, 2)
        return jnp.where(usable_q[:, None, None], picked, jnp.zeros_like(picked))

    own_dense = partial_of(own_hidden, own_cot)
    own_sent = blocks_of(own_dense, sent_q)
    own_kept = blocks_of(own_dense, kept_q)
    own_sent, own_kept, partner_cot = lax.optimization_barrier((own_sent, own_kept, partner_cot))
    partner_dense = partial_of(partner_hidden, partner_cot)

    def paired_of(own_blocks, table):
        total = own_blocks.astype(jnp.float32) + blocks_of(partner_dense, table).astype(jnp.float32)
        return total.astype(jnp.bfloat16)

    outgoing = paired_of(own_sent, sent_q)
    received = from_partner(outgoing, "mirror", 0)
    kept = paired_of(own_kept, kept_q)
    summed = (kept.astype(jnp.float32) + received.astype(jnp.float32)).astype(jnp.bfloat16)
    return summed.reshape(1, 1, -1, block_side, block_side)


def solution(mesh):
    placed = (
        P(None, "section", "mirror", None, "tp"),
        P(None, "section", "mirror", None, "tp"),
        P(None, "tp", None),
    )
    return jax.shard_map(
        body,
        mesh=mesh,
        in_specs=placed,
        out_specs=P("section", "tp", "mirror", None, None),
        check_vma=False,
    )
```

```python
import jax
import jax.numpy as jnp
from jax import lax
from jax.sharding import PartitionSpec as P

BLK = 128


def passed_along(block, axis, distance):
    devices = range(lax.axis_size(axis))
    route = [((i - distance) % len(devices), i) for i in devices]
    return lax.ppermute(block, axis, route)


def from_partner(value, axis, apart):
    mask = 2**apart
    pairs = [(source, source ^ mask) for source in range(lax.axis_size(axis))]
    return lax.ppermute(value, axis, pairs)


def slot_table(mask_local, slot_total):
    flat = mask_local.reshape(-1)
    running = jnp.cumsum(flat)
    positions = jnp.arange(slot_total, dtype=jnp.int32)
    targets = jnp.sum((running[None, :] <= positions[:, None]).astype(jnp.int32), axis=1)
    usable = positions < running[-1]
    targets = jnp.minimum(targets, flat.shape[0] - 1)
    columns_count = mask_local.shape[1]
    return (targets // columns_count, targets % columns_count, usable)


def body(hidden, incoming, block_mask):
    sections_total = lax.axis_size("section")
    half_count = sections_total // 2
    position = lax.axis_index("section")
    half_index = position // half_count
    section_index = position % half_count
    swap_bit = sections_total.bit_length() - 2
    block_side = BLK
    row_count = hidden.shape[3]
    ff_local = hidden.shape[4]

    own_hidden = hidden[:, 0, 0].reshape(2 * row_count, ff_local)
    arrived_all = jnp.stack(
        [
            passed_along(incoming[0, 0, 0], "section", -1),
            passed_along(incoming[1, 0, 0], "section", 1),
            passed_along(incoming[0, 0, 0], "section", -(half_count + 1)),
            passed_along(incoming[1, 0, 0], "section", half_count + 1),
        ]
    )
    partner_hidden = from_partner(own_hidden, "section", swap_bit)
    cot_all = lax.all_gather(arrived_all, "tp", axis=2, tiled=True)
    d_total = cot_all.shape[2]
    ffb = ff_local // block_side
    db = d_total // block_side

    mask_local = lax.dynamic_index_in_dim(block_mask, section_index, 0, keepdims=False)
    slot_total = mask_local.shape[0] * mask_local.shape[1] * 9 // 16
    slots_half = slot_total // 2
    slots_quarter = slots_half // 2
    block_rows, block_cols, usable = slot_table(mask_local, slot_total)
    mirror_index = lax.axis_index("mirror")

    def quarter(which):
        start = half_index * slots_half + which * slots_quarter
        pick = lambda table: lax.dynamic_slice_in_dim(table, start, slots_quarter, 0)
        return pick(block_rows), pick(block_cols), pick(usable)

    sent_q = quarter(1 - mirror_index)
    kept_q = quarter(mirror_index)

    def partial_of(hidden_rows, cot_rows):
        return jnp.einsum(
            "njd,nic->jidc",
            cot_rows.reshape(-1, db, block_side),
            hidden_rows.reshape(-1, ffb, block_side),
            preferred_element_type=jnp.float32,
        ).astype(jnp.bfloat16)

    def blocks_of(dense, table):
        rows_q, cols_q, usable_q = table
        picked = jnp.swapaxes(dense[cols_q, rows_q], 1, 2)
        return jnp.where(usable_q[:, None, None], picked, jnp.zeros_like(picked))

    own_dense = partial_of(own_hidden, cot_all[:2])
    own_sent = blocks_of(own_dense, sent_q)
    own_kept = blocks_of(own_dense, kept_q)
    own_sent, own_kept, partner_cot = lax.optimization_barrier((own_sent, own_kept, cot_all[2:]))
    partner_dense = partial_of(partner_hidden, partner_cot)

    def paired_of(own_blocks, table):
        total = own_blocks.astype(jnp.float32) + blocks_of(partner_dense, table).astype(jnp.float32)
        return total.astype(jnp.bfloat16)

    outgoing = paired_of(own_sent, sent_q)
    received = from_partner(outgoing, "mirror", 0)
    kept = paired_of(own_kept, kept_q)
    summed = (kept.astype(jnp.float32) + received.astype(jnp.float32)).astype(jnp.bfloat16)
    return summed.reshape(1, 1, -1, block_side, block_side)


def solution(mesh):
    placed = (
        P(None, "section", "mirror", None, "tp"),
        P(None, "section", "mirror", None, "tp"),
        P(None, "tp", None),
    )
    return jax.shard_map(
        body,
        mesh=mesh,
        in_specs=placed,
        out_specs=P("section", "tp", "mirror", None, None),
        check_vma=False,
    )
```

```python
import jax
import jax.numpy as jnp
from jax import lax
from jax.sharding import PartitionSpec as P

BLK = 128


def passed_along(block, axis, distance):
    devices = range(lax.axis_size(axis))
    route = [((i - distance) % len(devices), i) for i in devices]
    return lax.ppermute(block, axis, route)


def from_partner(value, axis, apart):
    mask = 2**apart
    pairs = [(source, source ^ mask) for source in range(lax.axis_size(axis))]
    return lax.ppermute(value, axis, pairs)


def slot_table(mask_local, slot_total):
    flat = mask_local.reshape(-1)
    running = jnp.cumsum(flat)
    positions = jnp.arange(slot_total, dtype=jnp.int32)
    targets = jnp.sum((running[None, :] <= positions[:, None]).astype(jnp.int32), axis=1)
    usable = positions < running[-1]
    targets = jnp.minimum(targets, flat.shape[0] - 1)
    columns_count = mask_local.shape[1]
    return (targets // columns_count, targets % columns_count, usable)


def body(hidden, incoming, block_mask):
    sections_total = lax.axis_size("section")
    half_count = sections_total // 2
    position = lax.axis_index("section")
    half_index = position // half_count
    section_index = position % half_count
    swap_bit = sections_total.bit_length() - 2
    block_side = BLK
    row_count = hidden.shape[3]
    ff_local = hidden.shape[4]

    own_hidden = hidden[:, 0, 0].reshape(2 * row_count, ff_local)
    arrived_all = jnp.stack(
        [
            passed_along(incoming[0, 0, 0], "section", -1),
            passed_along(incoming[1, 0, 0], "section", 1),
            passed_along(incoming[0, 0, 0], "section", -(half_count + 1)),
            passed_along(incoming[1, 0, 0], "section", half_count + 1),
        ]
    )
    partner_hidden = from_partner(own_hidden, "section", swap_bit)
    cot_all = lax.all_gather(arrived_all, "tp", axis=2, tiled=True)
    d_total = cot_all.shape[2]
    ffb = ff_local // block_side
    db = d_total // block_side

    mask_local = lax.dynamic_index_in_dim(block_mask, section_index, 0, keepdims=False)
    slot_total = mask_local.shape[0] * mask_local.shape[1] * 9 // 16
    slots_half = slot_total // 2
    slots_quarter = slots_half // 2
    block_rows, block_cols, usable = slot_table(mask_local, slot_total)
    mirror_index = lax.axis_index("mirror")

    def quarter(which):
        start = half_index * slots_half + which * slots_quarter
        pick = lambda table: lax.dynamic_slice_in_dim(table, start, slots_quarter, 0)
        return pick(block_rows), pick(block_cols), pick(usable)

    sent_q = quarter(1 - mirror_index)
    kept_q = quarter(mirror_index)

    def partial_of(hidden_rows, cot_rows):
        return jnp.einsum(
            "njd,nic->jidc",
            cot_rows.reshape(-1, db, block_side),
            hidden_rows.reshape(-1, ffb, block_side),
            preferred_element_type=jnp.float32,
        ).astype(jnp.bfloat16)

    def blocks_of(dense, table):
        rows_q, cols_q, usable_q = table
        picked = jnp.swapaxes(dense[cols_q, rows_q], 1, 2)
        return jnp.where(usable_q[:, None, None], picked, jnp.zeros_like(picked))

    own_dense = partial_of(own_hidden, cot_all[:2])
    own_sent = blocks_of(own_dense, sent_q)
    own_kept = blocks_of(own_dense, kept_q)
    partner_dense = partial_of(partner_hidden, cot_all[2:])

    def paired_of(own_blocks, table):
        total = own_blocks.astype(jnp.float32) + blocks_of(partner_dense, table).astype(jnp.float32)
        return total.astype(jnp.bfloat16)

    outgoing = paired_of(own_sent, sent_q)
    received = from_partner(outgoing, "mirror", 0)
    kept = paired_of(own_kept, kept_q)
    summed = (kept.astype(jnp.float32) + received.astype(jnp.float32)).astype(jnp.bfloat16)
    return summed.reshape(1, 1, -1, block_side, block_side)


def solution(mesh):
    placed = (
        P(None, "section", "mirror", None, "tp"),
        P(None, "section", "mirror", None, "tp"),
        P(None, "tp", None),
    )
    return jax.shard_map(
        body,
        mesh=mesh,
        in_specs=placed,
        out_specs=P("section", "tp", "mirror", None, None),
        check_vma=False,
    )
```

```python
import jax
import jax.numpy as jnp
from jax import lax
from jax.sharding import PartitionSpec as P

BLK = 128


def passed_along(block, axis, distance):
    devices = range(lax.axis_size(axis))
    route = [((i - distance) % len(devices), i) for i in devices]
    return lax.ppermute(block, axis, route)


def from_partner(value, axis, apart):
    mask = 2**apart
    pairs = [(source, source ^ mask) for source in range(lax.axis_size(axis))]
    return lax.ppermute(value, axis, pairs)


def slot_table(mask_local, slot_total):
    flat = mask_local.reshape(-1)
    running = jnp.cumsum(flat)
    positions = jnp.arange(slot_total, dtype=jnp.int32)
    targets = jnp.sum((running[None, :] <= positions[:, None]).astype(jnp.int32), axis=1)
    usable = positions < running[-1]
    targets = jnp.minimum(targets, flat.shape[0] - 1)
    columns_count = mask_local.shape[1]
    return (targets // columns_count, targets % columns_count, usable)


def body(hidden, incoming, block_mask):
    sections_total = lax.axis_size("section")
    half_count = sections_total // 2
    position = lax.axis_index("section")
    half_index = position // half_count
    section_index = position % half_count
    swap_bit = sections_total.bit_length() - 2
    block_side = BLK
    row_count = hidden.shape[3]
    ff_local = hidden.shape[4]

    own_hidden = hidden[:, 0, 0].reshape(2 * row_count, ff_local)
    arrived_all = jnp.stack(
        [
            passed_along(incoming[0, 0, 0], "section", -1),
            passed_along(incoming[1, 0, 0], "section", 1),
            passed_along(incoming[0, 0, 0], "section", -(half_count + 1)),
            passed_along(incoming[1, 0, 0], "section", half_count + 1),
        ]
    )
    partner_hidden = from_partner(own_hidden, "section", swap_bit)
    cot_all = lax.all_gather(arrived_all, "tp", axis=2, tiled=True)
    d_total = cot_all.shape[2]
    ffb = ff_local // block_side
    db = d_total // block_side

    mask_local = lax.dynamic_index_in_dim(block_mask, section_index, 0, keepdims=False)
    slot_total = mask_local.shape[0] * mask_local.shape[1] * 9 // 16
    slots_half = slot_total // 2
    slots_quarter = slots_half // 2
    block_rows, block_cols, usable = slot_table(mask_local, slot_total)
    mirror_index = lax.axis_index("mirror")

    def quarter(which):
        start = half_index * slots_half + which * slots_quarter
        pick = lambda table: lax.dynamic_slice_in_dim(table, start, slots_quarter, 0)
        return pick(block_rows), pick(block_cols), pick(usable)

    sent_q = quarter(1 - mirror_index)
    kept_q = quarter(mirror_index)

    def partial_of(hidden_rows, cot_rows):
        return jnp.einsum(
            "njd,nic->jidc",
            cot_rows.reshape(-1, db, block_side),
            hidden_rows.reshape(-1, ffb, block_side),
            preferred_element_type=jnp.float32,
        ).astype(jnp.bfloat16)

    def blocks_of(dense, table):
        rows_q, cols_q, usable_q = table
        picked = jnp.swapaxes(dense[cols_q, rows_q], 1, 2)
        return jnp.where(usable_q[:, None, None], picked, jnp.zeros_like(picked))

    own_dense = partial_of(own_hidden, cot_all[:2])
    own_kept = blocks_of(own_dense, kept_q)
    partner_dense = partial_of(partner_hidden, cot_all[2:])

    def paired_of(table):
        total = blocks_of(own_dense, table).astype(jnp.float32) + blocks_of(partner_dense, table).astype(jnp.float32)
        return total.astype(jnp.bfloat16)

    split = (slots_quarter + 1) // 2
    first_out = paired_of(tuple(part[:split] for part in sent_q))
    first_out, second_table = lax.optimization_barrier((first_out, tuple(part[split:] for part in sent_q)))
    first_back = from_partner(first_out, "mirror", 0)
    second_back = from_partner(paired_of(second_table), "mirror", 0)
    received = jnp.concatenate([first_back, second_back])
    kept = (own_kept.astype(jnp.float32) + blocks_of(partner_dense, kept_q).astype(jnp.float32)).astype(jnp.bfloat16)
    summed = (kept.astype(jnp.float32) + received.astype(jnp.float32)).astype(jnp.bfloat16)
    return summed.reshape(1, 1, -1, block_side, block_side)


def solution(mesh):
    placed = (
        P(None, "section", "mirror", None, "tp"),
        P(None, "section", "mirror", None, "tp"),
        P(None, "tp", None),
    )
    return jax.shard_map(
        body,
        mesh=mesh,
        in_specs=placed,
        out_specs=P("section", "tp", "mirror", None, None),
        check_vma=False,
    )
```

```python
import jax
import jax.numpy as jnp
from jax import lax
from jax.sharding import PartitionSpec as P

BLK = 128


def passed_along(block, axis, distance):
    devices = range(lax.axis_size(axis))
    route = [((i - distance) % len(devices), i) for i in devices]
    return lax.ppermute(block, axis, route)


def from_partner(value, axis, apart):
    mask = 2**apart
    pairs = [(source, source ^ mask) for source in range(lax.axis_size(axis))]
    return lax.ppermute(value, axis, pairs)


def slot_table(mask_local, slot_total):
    flat = mask_local.reshape(-1)
    running = jnp.cumsum(flat)
    positions = jnp.arange(slot_total, dtype=jnp.int32)
    targets = jnp.sum((running[None, :] <= positions[:, None]).astype(jnp.int32), axis=1)
    usable = positions < running[-1]
    targets = jnp.minimum(targets, flat.shape[0] - 1)
    columns_count = mask_local.shape[1]
    return (targets // columns_count, targets % columns_count, usable)


def body(hidden, incoming, block_mask):
    sections_total = lax.axis_size("section")
    half_count = sections_total // 2
    position = lax.axis_index("section")
    half_index = position // half_count
    section_index = position % half_count
    swap_bit = sections_total.bit_length() - 2
    block_side = BLK
    row_count = hidden.shape[3]
    ff_local = hidden.shape[4]

    own_hidden = hidden[:, 0, 0].reshape(2 * row_count, ff_local)
    arrived_all = jnp.stack(
        [
            passed_along(incoming[0, 0, 0], "section", -1),
            passed_along(incoming[1, 0, 0], "section", 1),
            passed_along(incoming[0, 0, 0], "section", -(half_count + 1)),
            passed_along(incoming[1, 0, 0], "section", half_count + 1),
        ]
    )
    partner_hidden = from_partner(own_hidden, "section", swap_bit)
    cot_all = lax.all_gather(arrived_all, "tp", axis=2, tiled=True)
    d_total = cot_all.shape[2]
    ffb = ff_local // block_side
    db = d_total // block_side

    mask_local = lax.dynamic_index_in_dim(block_mask, section_index, 0, keepdims=False)
    slot_total = mask_local.shape[0] * mask_local.shape[1] * 9 // 16
    slots_half = slot_total // 2
    slots_quarter = slots_half // 2
    block_rows, block_cols, usable = slot_table(mask_local, slot_total)
    mirror_index = lax.axis_index("mirror")

    def quarter(which):
        start = half_index * slots_half + which * slots_quarter
        pick = lambda table: lax.dynamic_slice_in_dim(table, start, slots_quarter, 0)
        return pick(block_rows), pick(block_cols), pick(usable)

    sent_q = quarter(1 - mirror_index)
    kept_q = quarter(mirror_index)

    def partial_of(hidden_rows, cot_rows):
        return jnp.einsum(
            "njd,nic->jidc",
            cot_rows.reshape(-1, db, block_side),
            hidden_rows.reshape(-1, ffb, block_side),
            preferred_element_type=jnp.float32,
        ).astype(jnp.bfloat16)

    def blocks_of(dense, table):
        rows_q, cols_q, usable_q = table
        picked = jnp.swapaxes(dense[cols_q, rows_q], 1, 2)
        return jnp.where(usable_q[:, None, None], picked, jnp.zeros_like(picked))

    dense = partial_of(jnp.concatenate([own_hidden, partner_hidden]), cot_all)
    received = from_partner(blocks_of(dense, sent_q), "mirror", 0)
    kept = blocks_of(dense, kept_q)
    summed = (kept.astype(jnp.float32) + received.astype(jnp.float32)).astype(jnp.bfloat16)
    return summed.reshape(1, 1, -1, block_side, block_side)


def solution(mesh):
    placed = (
        P(None, "section", "mirror", None, "tp"),
        P(None, "section", "mirror", None, "tp"),
        P(None, "tp", None),
    )
    return jax.shard_map(
        body,
        mesh=mesh,
        in_specs=placed,
        out_specs=P("section", "tp", "mirror", None, None),
        check_vma=False,
    )
```
